32 devices in a mesh: dp: 4 (over x, core), cent: 4 (over z), rep: 2 (over y).
Axes of the slice: x: 2, y: 2, z: 4, core: 2. Of those that a mesh axis runs over, the one named last changes fastest.
Arguments:
- points: bfloat16 [4096, 1024], P('dp'), may hold values from -6 to 6
- centroids: bfloat16 [8, 2048, 1024], P('rep', 'cent'), may hold values from -1.5 to 1.5
- counts: int32 [8, 4096], P('rep', 'dp'), may hold values from 0 to 5, as said below
Outputs:
- updated: bfloat16 [8, 2048, 1024], P('rep', 'cent', 'dp')
- bagged_score: float32 [4096], P('dp')
The draws below stay inside these ranges and needn't reach their ends.
Inputs may be any that keep to these rules, and one draw needn't show every extreme that they name: `counts`: in every replicate some point has count 5.
All inputs are finite; a program needn't handle non-finite values.
Results may differ from the reference program's by a relative error of at most 0.0045.
Values sent between devices are 32-bit elements; how exact they have to be, the bound alone decides.
No kernel may reach another device: no remote copies, remote signals or barrier semaphores. Data moves between devices by JAX's collectives and lax.ppermute only.
A program may use at most 64 MiB of HBM per device.

```python
import math
import jax
import jax.numpy as jnp
import numpy as np
from jax import lax

D = 1024
K = 2048
REPS = 8
POINTS = 4096


def drawn_layout():
    replica = np.repeat(np.arange(REPS), 8)
    member = np.tile(np.arange(8), REPS)
    target = 110.0 + 20.0 * member
    amplitude = np.minimum(np.floor(16.0 * (target / D + 1.125) / 1.5 + 0.5) / 16.0, 6.0)
    grid = np.arange(-12, 13) / 8.0
    altered = np.zeros(member.shape[0])
    for index in range(member.shape[0]):
        gaps = (1.5 - grid) * (amplitude[index] - (1.5 + grid) / 2.0)
        altered[index] = grid[np.argmin(np.abs(gaps - 2.0))]
    return (replica, amplitude.astype(np.float32), altered.astype(np.float32))


def drawn_points(key):
    order = jax.random.permutation(jax.random.fold_in(key, 16), POINTS)
    return order[:REPS * 8]


def pick_rows(branch_key):
    return jax.random.permutation(branch_key, K // 2)[:8]


def drawn_rows(key):
    branch_keys = jax.random.split(jax.random.fold_in(key, 17), REPS)
    halves = jax.vmap(pick_rows)(branch_keys)
    first_row = 2 * halves.reshape(-1)
    return (first_row, first_row + 1)


def planted_signs(key):
    bits = jax.random.bernoulli(jax.random.fold_in(key, 15), 0.5, (REPS * 8, D))
    return jnp.where(bits, 1.0, -1.0).astype(jnp.float32)


def base_points(key):
    inner = jax.random.fold_in(key, 11)
    source = jnp.clip(jax.random.normal(inner, (POINTS, D), jnp.float32), -6.0, 6.0)
    replica, amplitude, altered = drawn_layout()
    picked = drawn_points(key)
    signs = planted_signs(key)
    return source.at[picked].set(jnp.asarray(amplitude)[:, None] * signs)


def draw_points(key, part):
    return base_points(key).astype(jnp.bfloat16)


def draw_centroids(key, part):
    noise = 0.1 * jnp.clip(jax.random.normal(jax.random.fold_in(key, 12), (REPS, K, D), jnp.float32), -6.0, 6.0)
    replica, amplitude, altered = drawn_layout()
    first_row, second_row = drawn_rows(key)
    signs = planted_signs(key)
    first_values = 1.5 * signs
    second_values = first_values.at[:, 0].set(jnp.asarray(altered) * signs[:, 0])
    noise = noise.at[replica, first_row].set(first_values)
    noise = noise.at[replica, second_row].set(second_values)
    return noise.astype(jnp.bfloat16)


def draw_counts(key, part):
    trials = jax.random.randint(jax.random.fold_in(key, 13), (16, REPS, POINTS), 0, 16)
    drawn = jnp.minimum(jnp.sum((trials == 0).astype(jnp.int32), axis=0), 5)
    spots = jax.random.randint(jax.random.fold_in(key, 14), (REPS,), 0, POINTS)
    return drawn.at[jnp.arange(REPS), spots].set(5)


def setup_inputs(seed: int = 0) -> dict:
    key_list = jax.random.split(jax.random.key(seed), 4)
    return {
        "points": draw_points(jax.random.fold_in(key_list[3], 71), 0),
        "centroids": draw_centroids(jax.random.fold_in(key_list[3], 71), 0),
        "counts": draw_counts(jax.random.fold_in(key_list[3], 71), 0),
    }


prior_weight = 1.0


def reference(points, centroids, counts):
    def one_replicate(pair):
        center, weight = pair
        squares = jnp.sum(jnp.square(center.astype(jnp.float32)), axis=1)
        logits = jnp.dot(points, center.T, preferred_element_type=jnp.float32) - 0.5 * squares[None, :]
        row_top = jnp.max(logits, axis=1, keepdims=True)
        expo = jnp.exp(logits - row_top)
        row_total = jnp.sum(expo, axis=1, keepdims=True)
        weighted = (expo / row_total * weight[:, None].astype(jnp.float32)).astype(jnp.bfloat16)
        moment_sums = jnp.dot(weighted.T, points, preferred_element_type=jnp.float32)
        cluster_mass = jnp.sum(weighted.astype(jnp.float32), axis=0)
        updated = ((moment_sums + prior_weight * center.astype(jnp.float32)) / (cluster_mass + prior_weight)[:, None]).astype(jnp.bfloat16)
        log_total = row_top[:, 0] + jnp.log(row_total[:, 0])
        return updated, log_total

    updated, log_total = lax.map(one_replicate, (centroids, counts))
    bagged_score = jnp.sum(log_total, axis=0) / REPS - math.log(K)
    return updated, bagged_score
```

```python
import math

import jax
import jax.numpy as jnp
from jax import lax
from jax.sharding import PartitionSpec as P

prior_weight = 1.0


def _all_gather_shifts(x, axis):
    n = lax.axis_size(axis)
    outs = [x]
    for s in range(1, n):
        outs.append(lax.ppermute(x, axis, [(i, (i + s) % n) for i in range(n)]))
    return jnp.stack(outs)


def _all_reduce_doubling(x, axis):
    n = lax.axis_size(axis)
    if n & (n - 1):
        return lax.psum(x, axis)
    b = 1
    while b < n:
        x = x + lax.ppermute(x, axis, [(i, i ^ b) for i in range(n)])
        b *= 2
    return x


def _reduce_scatter_halving(pieces, axis):
    n = lax.axis_size(axis)
    index = lax.axis_index(axis)
    b = 1
    while b < n:
        m = pieces.shape[0] // 2
        view = pieces.reshape((m, 2) + pieces.shape[1:])
        mine = (index // b) % 2
        keep = lax.dynamic_index_in_dim(view, mine, axis=1, keepdims=False)
        send = lax.dynamic_index_in_dim(view, 1 - mine, axis=1, keepdims=False)
        pieces = keep + lax.ppermute(send, axis, [(i, i ^ b) for i in range(n)])
        b *= 2
    return pieces[0]


def shards(points, centroids, counts):
    rep_local, cent_local, features = centroids.shape
    ndp = lax.axis_size("dp")
    slab_width = features // ndp
    position = lax.axis_index("dp")
    points3 = points.reshape(points.shape[0], ndp, slab_width)
    updated = []
    log_total = []
    for r in range(rep_local):
        center = centroids[r]
        squares = jnp.sum(jnp.square(center.astype(jnp.float32)), axis=1)
        logits = (
            jnp.dot(points, center.T, preferred_element_type=jnp.float32) - 0.5 * squares[None, :]
        )
        local_top = jnp.max(logits, axis=1)
        local_total = jnp.sum(jnp.exp(logits - local_top[:, None]), axis=1)
        gathered = _all_gather_shifts(jnp.stack([local_top, local_total]), "cent")
        row_top = jnp.max(gathered[:, 0], axis=0)
        row_total = jnp.sum(gathered[:, 1] * jnp.exp(gathered[:, 0] - row_top[None, :]), axis=0)
        weights = counts[r].astype(jnp.float32)
        weighted = (
            jnp.exp(logits - row_top[:, None]) / row_total[:, None] * weights[:, None]
        ).astype(jnp.bfloat16)
        mass = _all_reduce_doubling(jnp.sum(weighted.astype(jnp.float32), axis=0), "dp")
        pieces = jnp.einsum("nk,njd->jkd", weighted, points3, preferred_element_type=jnp.float32)
        moments = _reduce_scatter_halving(pieces, "dp")
        own_slice = lax.dynamic_slice_in_dim(center, position * slab_width, slab_width, 1).astype(
            jnp.float32
        )
        updated.append(
            ((moments + prior_weight * own_slice) / (mass[:, None] + prior_weight)).astype(
                jnp.bfloat16
            )
        )
        log_total.append(row_top + jnp.log(row_total))
    updated = jnp.stack(updated)
    summed = _all_reduce_doubling(sum(log_total), "rep")
    replicas = rep_local * lax.axis_size("rep")
    clusters = cent_local * lax.axis_size("cent")
    bagged_score = summed / replicas - math.log(clusters)
    return (updated, bagged_score)


def solution(mesh):
    return jax.shard_map(
        shards,
        mesh=mesh,
        in_specs=(P("dp", None), P("rep", "cent", None), P("rep", "dp")),
        out_specs=(P("rep", "cent", "dp"), P("dp")),
        check_vma=False,
    )
```

```python
import math

import jax
import jax.numpy as jnp
from jax import lax
from jax.sharding import PartitionSpec as P

prior_weight = 1.0


def _all_gather_shifts(x, axis):
    n = lax.axis_size(axis)
    outs = [x]
    for s in range(1, n):
        outs.append(lax.ppermute(x, axis, [(i, (i + s) % n) for i in range(n)]))
    return jnp.stack(outs)


def _all_reduce_doubling(x, axis):
    n = lax.axis_size(axis)
    if n & (n - 1):
        return lax.psum(x, axis)
    b = 1
    while b < n:
        x = x + lax.ppermute(x, axis, [(i, i ^ b) for i in range(n)])
        b *= 2
    return x


def _halving_step(pieces, axis, b):
    n = lax.axis_size(axis)
    m = pieces.shape[0] // 2
    view = pieces.reshape((m, 2) + pieces.shape[1:])
    mine = (lax.axis_index(axis) // b) % 2
    keep = lax.dynamic_index_in_dim(view, mine, axis=1, keepdims=False)
    send = lax.dynamic_index_in_dim(view, 1 - mine, axis=1, keepdims=False)
    return keep + lax.ppermute(send, axis, [(i, i ^ b) for i in range(n)])


def _halving_rest(pieces, axis, b):
    n = lax.axis_size(axis)
    while b < n:
        pieces = _halving_step(pieces, axis, b)
        b *= 2
    return pieces[0]


def shards(points, centroids, counts):
    rep_local, cent_local, features = centroids.shape
    ndp = lax.axis_size("dp")
    slab_width = features // ndp
    position = lax.axis_index("dp")
    points3 = points.reshape(points.shape[0], ndp, slab_width)
    moments = []
    masses = []
    log_total = []
    pending = None
    for r in range(rep_local):
        center = centroids[r]
        squares = jnp.sum(jnp.square(center.astype(jnp.float32)), axis=1)
        logits = (
            jnp.dot(points, center.T, preferred_element_type=jnp.float32) - 0.5 * squares[None, :]
        )
        local_top = jnp.max(logits, axis=1)
        local_total = jnp.sum(jnp.exp(logits - local_top[:, None]), axis=1)
        gathered = _all_gather_shifts(jnp.stack([local_top, local_total]), "cent")
        row_top = jnp.max(gathered[:, 0], axis=0)
        row_total = jnp.sum(gathered[:, 1] * jnp.exp(gathered[:, 0] - row_top[None, :]), axis=0)
        weights = counts[r].astype(jnp.float32)
        weighted = (
            jnp.exp(logits - row_top[:, None]) / row_total[:, None] * weights[:, None]
        ).astype(jnp.bfloat16)
        masses.append(jnp.sum(weighted.astype(jnp.float32), axis=0))
        if pending is not None:
            weighted, pending = lax.optimization_barrier((weighted, pending))
            moments.append(_halving_rest(pending, "dp", 2))
        pieces = jnp.einsum("nk,njd->jkd", weighted, points3, preferred_element_type=jnp.float32)
        pending = _halving_step(pieces, "dp", 1) if ndp > 1 else pieces
        log_total.append(row_top + jnp.log(row_total))
    moments.append(_halving_rest(pending, "dp", 2))
    mass = _all_reduce_doubling(jnp.stack(masses), "dp")
    own_slice = lax.dynamic_slice_in_dim(centroids, position * slab_width, slab_width, 2).astype(
        jnp.float32
    )
    updated = (
        (jnp.stack(moments) + prior_weight * own_slice) / (mass[:, :, None] + prior_weight)
    ).astype(jnp.bfloat16)
    summed = _all_reduce_doubling(sum(log_total), "rep")
    replicas = rep_local * lax.axis_size("rep")
    clusters = cent_local * lax.axis_size("cent")
    bagged_score = summed / replicas - math.log(clusters)
    return (updated, bagged_score)


def solution(mesh):
    return jax.shard_map(
        shards,
        mesh=mesh,
        in_specs=(P("dp", None), P("rep", "cent", None), P("rep", "dp")),
        out_specs=(P("rep", "cent", "dp"), P("dp")),
        check_vma=False,
    )
```

```python
import math

import jax
import jax.numpy as jnp
from jax import lax
from jax.sharding import PartitionSpec as P

prior_weight = 1.0

LAG = 1


def _all_gather_shifts(x, axis):
    n = lax.axis_size(axis)
    outs = [x]
    for s in range(1, n):
        outs.append(lax.ppermute(x, axis, [(i, (i + s) % n) for i in range(n)]))
    return jnp.stack(outs)


def _all_reduce_doubling(x, axis):
    n = lax.axis_size(axis)
    if n & (n - 1):
        return lax.psum(x, axis)
    b = 1
    while b < n:
        x = x + lax.ppermute(x, axis, [(i, i ^ b) for i in range(n)])
        b *= 2
    return x


def _halving_step(pieces, axis, b):
    n = lax.axis_size(axis)
    m = pieces.shape[0] // 2
    view = pieces.reshape((m, 2) + pieces.shape[1:])
    mine = (lax.axis_index(axis) // b) % 2
    keep = lax.dynamic_index_in_dim(view, mine, axis=1, keepdims=False)
    send = lax.dynamic_index_in_dim(view, 1 - mine, axis=1, keepdims=False)
    return keep + lax.ppermute(send, axis, [(i, i ^ b) for i in range(n)])


def _halving_rest(pieces, axis, b):
    n = lax.axis_size(axis)
    while b < n:
        pieces = _halving_step(pieces, axis, b)
        b *= 2
    return pieces[0]


def shards(points, centroids, counts):
    rep_local, cent_local, features = centroids.shape
    ndp = lax.axis_size("dp")
    slab_width = features // ndp
    position = lax.axis_index("dp")
    points3 = points.reshape(points.shape[0], ndp, slab_width)
    moments = []
    masses = []
    log_total = []
    pending = []
    for r in range(rep_local):
        center = centroids[r]
        squares = jnp.sum(jnp.square(center.astype(jnp.float32)), axis=1)
        logits = (
            jnp.dot(points, center.T, preferred_element_type=jnp.float32) - 0.5 * squares[None, :]
        )
        local_top = jnp.max(logits, axis=1)
        local_total = jnp.sum(jnp.exp(logits - local_top[:, None]), axis=1)
        gathered = _all_gather_shifts(jnp.stack([local_top, local_total]), "cent")
        row_top = jnp.max(gathered[:, 0], axis=0)
        row_total = jnp.sum(gathered[:, 1] * jnp.exp(gathered[:, 0] - row_top[None, :]), axis=0)
        weights = counts[r].astype(jnp.float32)
        weighted = (
            jnp.exp(logits - row_top[:, None]) / row_total[:, None] * weights[:, None]
        ).astype(jnp.bfloat16)
        masses.append(jnp.sum(weighted.astype(jnp.float32), axis=0))
        if pending:
            weighted, first = lax.optimization_barrier((weighted, pending[-1]))
            pending[-1] = _halving_rest(first, "dp", 2)
            if len(pending) > LAG:
                weighted, done = lax.optimization_barrier((weighted, pending[-1 - LAG]))
                moments.append(done)
        pieces = jnp.einsum("nk,njd->jkd", weighted, points3, preferred_element_type=jnp.float32)
        pending.append(_halving_step(pieces, "dp", 1) if ndp > 1 else pieces)
        log_total.append(row_top + jnp.log(row_total))
    pending[-1] = _halving_rest(pending[-1], "dp", 2)
    moments.extend(pending[len(moments):])
    mass = _all_reduce_doubling(jnp.stack(masses), "dp")
    own_slice = lax.dynamic_slice_in_dim(centroids, position * slab_width, slab_width, 2).astype(
        jnp.float32
    )
    updated = (
        (jnp.stack(moments) + prior_weight * own_slice) / (mass[:, :, None] + prior_weight)
    ).astype(jnp.bfloat16)
    summed = _all_reduce_doubling(sum(log_total), "rep")
    replicas = rep_local * lax.axis_size("rep")
    clusters = cent_local * lax.axis_size("cent")
    bagged_score = summed / replicas - math.log(clusters)
    return (updated, bagged_score)


def solution(mesh):
    return jax.shard_map(
        shards,
        mesh=mesh,
        in_specs=(P("dp", None), P("rep", "cent", None), P("rep", "dp")),
        out_specs=(P("rep", "cent", "dp"), P("dp")),
        check_vma=False,
    )
```

```python
import math

import jax
import jax.numpy as jnp
from jax import lax
from jax.sharding import PartitionSpec as P

prior_weight = 1.0

LAG = 1


def _softmax_stats(top, total, axis):
    n = lax.axis_size(axis)
    if n & (n - 1):
        row_top = lax.pmax(top, axis)
        return row_top, lax.psum(total * jnp.exp(top - row_top), axis)
    b = 1
    while b < n:
        other = lax.ppermute(jnp.stack([top, total]), axis, [(i, i ^ b) for i in range(n)])
        new_top = jnp.maximum(top, other[0])
        total = total * jnp.exp(top - new_top) + other[1] * jnp.exp(other[0] - new_top)
        top = new_top
        b *= 2
    return top, total


def _all_reduce_doubling(x, axis):
    n = lax.axis_size(axis)
    if n & (n - 1):
        return lax.psum(x, axis)
    b = 1
    while b < n:
        x = x + lax.ppermute(x, axis, [(i, i ^ b) for i in range(n)])
        b *= 2
    return x


def _halving_step(pieces, axis, b):
    n = lax.axis_size(axis)
    m = pieces.shape[0] // 2
    view = pieces.reshape((m, 2) + pieces.shape[1:])
    mine = (lax.axis_index(axis) // b) % 2
    keep = lax.dynamic_index_in_dim(view, mine, axis=1, keepdims=False)
    send = lax.dynamic_index_in_dim(view, 1 - mine, axis=1, keepdims=False)
    return keep + lax.ppermute(send, axis, [(i, i ^ b) for i in range(n)])


def _halving_rest(pieces, axis, b):
    n = lax.axis_size(axis)
    while b < n:
        pieces = _halving_step(pieces, axis, b)
        b *= 2
    return pieces[0]


def shards(points, centroids, counts):
    rep_local, cent_local, features = centroids.shape
    ndp = lax.axis_size("dp")
    slab_width = features // ndp
    position = lax.axis_index("dp")
    points3 = points.reshape(points.shape[0], ndp, slab_width)
    moments = []
    masses = []
    log_total = []
    pending = []
    squares = jnp.sum(jnp.square(centroids.astype(jnp.float32)), axis=2)
    all_logits = []
    for r in range(rep_local):
        all_logits.append(
            jnp.dot(points, centroids[r].T, preferred_element_type=jnp.float32)
            - 0.5 * squares[r][None, :]
        )
    local_top = jnp.stack([jnp.max(l, axis=1) for l in all_logits])
    local_total = jnp.stack(
        [jnp.sum(jnp.exp(l - t[:, None]), axis=1) for l, t in zip(all_logits, local_top)]
    )
    tops, totals = _softmax_stats(local_top, local_total, "cent")
    for r in range(rep_local):
        logits = all_logits[r]
        row_top = tops[r]
        row_total = totals[r]
        weights = counts[r].astype(jnp.float32)
        weighted = (
            jnp.exp(logits - row_top[:, None]) / row_total[:, None] * weights[:, None]
        ).astype(jnp.bfloat16)
        masses.append(jnp.sum(weighted.astype(jnp.float32), axis=0))
        if pending:
            weighted, first = lax.optimization_barrier((weighted, pending[-1]))
            pending[-1] = _halving_rest(first, "dp", 2)
            if len(pending) > LAG:
                weighted, done = lax.optimization_barrier((weighted, pending[-1 - LAG]))
                moments.append(done)
        pieces = jnp.einsum("nk,njd->jkd", weighted, points3, preferred_element_type=jnp.float32)
        pending.append(_halving_step(pieces, "dp", 1) if ndp > 1 else pieces)
        log_total.append(row_top + jnp.log(row_total))
    pending[-1] = _halving_rest(pending[-1], "dp", 2)
    moments.extend(pending[len(moments):])
    mass = _all_reduce_doubling(jnp.stack(masses), "dp")
    own_slice = lax.dynamic_slice_in_dim(centroids, position * slab_width, slab_width, 2).astype(
        jnp.float32
    )
    updated = (
        (jnp.stack(moments) + prior_weight * own_slice) / (mass[:, :, None] + prior_weight)
    ).astype(jnp.bfloat16)
    summed = _all_reduce_doubling(sum(log_total), "rep")
    replicas = rep_local * lax.axis_size("rep")
    clusters = cent_local * lax.axis_size("cent")
    bagged_score = summed / replicas - math.log(clusters)
    return (updated, bagged_score)


def solution(mesh):
    return jax.shard_map(
        shards,
        mesh=mesh,
        in_specs=(P("dp", None), P("rep", "cent", None), P("rep", "dp")),
        out_specs=(P("rep", "cent", "dp"), P("dp")),
        check_vma=False,
    )
```

```python
import math

import jax
import jax.numpy as jnp
from jax import lax
from jax.sharding import PartitionSpec as P

prior_weight = 1.0

LAG = 1


def _softmax_stats(top, total, axis):
    n = lax.axis_size(axis)
    if n & (n - 1):
        row_top = lax.pmax(top, axis)
        return row_top, lax.psum(total * jnp.exp(top - row_top), axis)
    b = 1
    while b < n:
        other = lax.ppermute(jnp.stack([top, total]), axis, [(i, i ^ b) for i in range(n)])
        new_top = jnp.maximum(top, other[0])
        total = total * jnp.exp(top - new_top) + other[1] * jnp.exp(other[0] - new_top)
        top = new_top
        b *= 2
    return top, total


def _all_reduce_doubling(x, axis):
    n = lax.axis_size(axis)
    if n & (n - 1):
        return lax.psum(x, axis)
    b = 1
    while b < n:
        x = x + lax.ppermute(x, axis, [(i, i ^ b) for i in range(n)])
        b *= 2
    return x


def _halving_order(axis):
    n = lax.axis_size(axis)
    bits = n.bit_length() - 1
    index = lax.axis_index(axis)
    order = []
    for p in range(n):
        j = 0
        for b in range(bits):
            flip = 1 - ((p >> (bits - 1 - b)) & 1)
            j = j + ((((index >> b) & 1) ^ flip) << b)
        order.append(j)
    return order


def _halving_step(pieces, axis, b):
    n = lax.axis_size(axis)
    m = pieces.shape[0] // 2
    return pieces[m:] + lax.ppermute(pieces[:m], axis, [(i, i ^ b) for i in range(n)])


def _halving_rest(pieces, axis, b):
    n = lax.axis_size(axis)
    while b < n:
        pieces = _halving_step(pieces, axis, b)
        b *= 2
    return pieces[0]


def shards(points, centroids, counts):
    rep_local, cent_local, features = centroids.shape
    ndp = lax.axis_size("dp")
    slab_width = features // ndp
    position = lax.axis_index("dp")
    points3 = jnp.stack(
        [
            lax.dynamic_slice_in_dim(points, j * slab_width, slab_width, 1)
            for j in _halving_order("dp")
        ],
        axis=1,
    )
    moments = []
    masses = []
    log_total = []
    pending = []
    squares = jnp.sum(jnp.square(centroids.astype(jnp.float32)), axis=2)
    all_logits = []
    for r in range(rep_local):
        all_logits.append(
            jnp.dot(points, centroids[r].T, preferred_element_type=jnp.float32)
            - 0.5 * squares[r][None, :]
        )
    local_top = jnp.stack([jnp.max(l, axis=1) for l in all_logits])
    local_total = jnp.stack(
        [jnp.sum(jnp.exp(l - t[:, None]), axis=1) for l, t in zip(all_logits, local_top)]
    )
    tops, totals = _softmax_stats(local_top, local_total, "cent")
    for r in range(rep_local):
        logits = all_logits[r]
        row_top = tops[r]
        row_total = totals[r]
        weights = counts[r].astype(jnp.float32)
        weighted = (
            jnp.exp(logits - row_top[:, None]) / row_total[:, None] * weights[:, None]
        ).astype(jnp.bfloat16)
        masses.append(jnp.sum(weighted.astype(jnp.float32), axis=0))
        if pending:
            weighted, first = lax.optimization_barrier((weighted, pending[-1]))
            pending[-1] = _halving_rest(first, "dp", 2)
            if len(pending) > LAG:
                weighted, done = lax.optimization_barrier((weighted, pending[-1 - LAG]))
                moments.append(done)
        pieces = jnp.einsum("nk,njd->jkd", weighted, points3, preferred_element_type=jnp.float32)
        pending.append(_halving_step(pieces, "dp", 1) if ndp > 1 else pieces)
        log_total.append(row_top + jnp.log(row_total))
    pending[-1] = _halving_rest(pending[-1], "dp", 2)
    moments.extend(pending[len(moments):])
    mass = _all_reduce_doubling(jnp.stack(masses), "dp")
    own_slice = lax.dynamic_slice_in_dim(centroids, position * slab_width, slab_width, 2).astype(
        jnp.float32
    )
    updated = (
        (jnp.stack(moments) + prior_weight * own_slice) / (mass[:, :, None] + prior_weight)
    ).astype(jnp.bfloat16)
    summed = _all_reduce_doubling(sum(log_total), "rep")
    replicas = rep_local * lax.axis_size("rep")
    clusters = cent_local * lax.axis_size("cent")
    bagged_score = summed / replicas - math.log(clusters)
    return (updated, bagged_score)


def solution(mesh):
    return jax.shard_map(
        shards,
        mesh=mesh,
        in_specs=(P("dp", None), P("rep", "cent", None), P("rep", "dp")),
        out_specs=(P("rep", "cent", "dp"), P("dp")),
        check_vma=False,
    )
```

```python
import math

import jax
import jax.numpy as jnp
from jax import lax
from jax.sharding import PartitionSpec as P

prior_weight = 1.0

LAG = 1


def _softmax_stats(top, total, axis):
    n = lax.axis_size(axis)
    index = lax.axis_index(axis)
    stats = jnp.stack([top, total])
    shifted = [stats]
    for s in range(1, n):
        shifted.append(lax.ppermute(stats, axis, [(i, (i + s) % n) for i in range(n)]))
    shifted = jnp.stack(shifted)
    ordered = jnp.take(shifted, (index - jnp.arange(n)) % n, axis=0)
    row_top = jnp.max(ordered[:, 0], axis=0)
    row_total = jnp.sum(ordered[:, 1] * jnp.exp(ordered[:, 0] - row_top[None]), axis=0)
    return row_top, row_total


def _all_reduce_doubling(x, axis):
    n = lax.axis_size(axis)
    if n & (n - 1):
        return lax.psum(x, axis)
    b = 1
    while b < n:
        x = x + lax.ppermute(x, axis, [(i, i ^ b) for i in range(n)])
        b *= 2
    return x


def _halving_order(axis):
    n = lax.axis_size(axis)
    bits = n.bit_length() - 1
    index = lax.axis_index(axis)
    order = []
    for p in range(n):
        j = 0
        for b in range(bits):
            flip = 1 - ((p >> (bits - 1 - b)) & 1)
            j = j + ((((index >> b) & 1) ^ flip) << b)
        order.append(j)
    return order


def _halving_step(pieces, axis, b):
    n = lax.axis_size(axis)
    m = pieces.shape[0] // 2
    return pieces[m:] + lax.ppermute(pieces[:m], axis, [(i, i ^ b) for i in range(n)])


def _halving_rest(pieces, axis, b):
    n = lax.axis_size(axis)
    while b < n:
        pieces = _halving_step(pieces, axis, b)
        b *= 2
    return pieces[0]


def shards(points, centroids, counts):
    rep_local, cent_local, features = centroids.shape
    ndp = lax.axis_size("dp")
    slab_width = features // ndp
    position = lax.axis_index("dp")
    points3 = jnp.stack(
        [
            lax.dynamic_slice_in_dim(points, j * slab_width, slab_width, 1)
            for j in _halving_order("dp")
        ],
        axis=1,
    )
    moments = []
    masses = []
    log_total = []
    pending = []
    squares = jnp.sum(jnp.square(centroids.astype(jnp.float32)), axis=2)
    all_logits = []
    for r in range(rep_local):
        all_logits.append(
            jnp.dot(points, centroids[r].T, preferred_element_type=jnp.float32)
            - 0.5 * squares[r][None, :]
        )
    local_top = jnp.stack([jnp.max(l, axis=1) for l in all_logits])
    local_total = jnp.stack(
        [jnp.sum(jnp.exp(l - t[:, None]), axis=1) for l, t in zip(all_logits, local_top)]
    )
    tops, totals = _softmax_stats(local_top, local_total, "cent")
    for r in range(rep_local):
        logits = all_logits[r]
        row_top = tops[r]
        row_total = totals[r]
        weights = counts[r].astype(jnp.float32)
        weighted = (
            jnp.exp(logits - row_top[:, None]) / row_total[:, None] * weights[:, None]
        ).astype(jnp.bfloat16)
        masses.append(jnp.sum(weighted.astype(jnp.float32), axis=0))
        if pending:
            weighted, first = lax.optimization_barrier((weighted, pending[-1]))
            pending[-1] = _halving_rest(first, "dp", 2)
            if len(pending) > LAG:
                weighted, done = lax.optimization_barrier((weighted, pending[-1 - LAG]))
                moments.append(done)
        pieces = jnp.einsum("nk,njd->jkd", weighted, points3, preferred_element_type=jnp.float32)
        pending.append(_halving_step(pieces, "dp", 1) if ndp > 1 else pieces)
        log_total.append(row_top + jnp.log(row_total))
    pending[-1] = _halving_rest(pending[-1], "dp", 2)
    moments.extend(pending[len(moments):])
    mass = _all_reduce_doubling(jnp.stack(masses), "dp")
    own_slice = lax.dynamic_slice_in_dim(centroids, position * slab_width, slab_width, 2).astype(
        jnp.float32
    )
    updated = (
        (jnp.stack(moments) + prior_weight * own_slice) / (mass[:, :, None] + prior_weight)
    ).astype(jnp.bfloat16)
    summed = _all_reduce_doubling(sum(log_total), "rep")
    replicas = rep_local * lax.axis_size("rep")
    clusters = cent_local * lax.axis_size("cent")
    bagged_score = summed / replicas - math.log(clusters)
    return (updated, bagged_score)


def solution(mesh):
    return jax.shard_map(
        shards,
        mesh=mesh,
        in_specs=(P("dp", None), P("rep", "cent", None), P("rep", "dp")),
        out_specs=(P("rep", "cent", "dp"), P("dp")),
        check_vma=False,
    )
```

```python
import math

import jax
import jax.numpy as jnp
from jax import lax
from jax.sharding import PartitionSpec as P

prior_weight = 1.0

GROUP = 2


def _softmax_stats(top, total, axis):
    n = lax.axis_size(axis)
    index = lax.axis_index(axis)
    stats = jnp.stack([top, total])
    shifted = [stats]
    for s in range(1, n):
        shifted.append(lax.ppermute(stats, axis, [(i, (i + s) % n) for i in range(n)]))
    shifted = jnp.stack(shifted)
    ordered = jnp.take(shifted, (index - jnp.arange(n)) % n, axis=0)
    row_top = jnp.max(ordered[:, 0], axis=0)
    row_total = jnp.sum(ordered[:, 1] * jnp.exp(ordered[:, 0] - row_top[None]), axis=0)
    return row_top, row_total


def _all_reduce_doubling(x, axis):
    n = lax.axis_size(axis)
    if n & (n - 1):
        return lax.psum(x, axis)
    b = 1
    while b < n:
        x = x + lax.ppermute(x, axis, [(i, i ^ b) for i in range(n)])
        b *= 2
    return x


def _halving_order(axis):
    n = lax.axis_size(axis)
    bits = n.bit_length() - 1
    index = lax.axis_index(axis)
    order = []
    for p in range(n):
        j = 0
        for b in range(bits):
            flip = 1 - ((p >> (bits - 1 - b)) & 1)
            j = j + ((((index >> b) & 1) ^ flip) << b)
        order.append(j)
    return order


def _halving_step(pieces, axis, b):
    n = lax.axis_size(axis)
    m = pieces.shape[0] // 2
    return pieces[m:] + lax.ppermute(pieces[:m], axis, [(i, i ^ b) for i in range(n)])


def _halving_rest(pieces, axis, b):
    n = lax.axis_size(axis)
    while b < n:
        pieces = _halving_step(pieces, axis, b)
        b *= 2
    return pieces[0]


def shards(points, centroids, counts):
    rep_local, cent_local, features = centroids.shape
    ndp = lax.axis_size("dp")
    slab_width = features // ndp
    position = lax.axis_index("dp")
    points3 = jnp.stack(
        [
            lax.dynamic_slice_in_dim(points, j * slab_width, slab_width, 1)
            for j in _halving_order("dp")
        ],
        axis=1,
    )
    moments = []
    masses = []
    log_total = []
    pending = []
    squares = jnp.sum(jnp.square(centroids.astype(jnp.float32)), axis=2)
    all_logits = []
    for r in range(rep_local):
        all_logits.append(
            jnp.dot(points, centroids[r].T, preferred_element_type=jnp.float32)
            - 0.5 * squares[r][None, :]
        )
    local_top = jnp.stack([jnp.max(l, axis=1) for l in all_logits])
    local_total = jnp.stack(
        [jnp.sum(jnp.exp(l - t[:, None]), axis=1) for l, t in zip(all_logits, local_top)]
    )
    tops, totals = _softmax_stats(local_top, local_total, "cent")
    moments = []
    group_firsts = []
    first = None
    second = None
    for r in range(rep_local):
        logits = all_logits[r]
        row_top = tops[r]
        row_total = totals[r]
        weights = counts[r].astype(jnp.float32)
        weighted = (
            jnp.exp(logits - row_top[:, None]) / row_total[:, None] * weights[:, None]
        ).astype(jnp.bfloat16)
        masses.append(jnp.sum(weighted.astype(jnp.float32), axis=0))
        opened = None
        if first is not None:
            weighted, first = lax.optimization_barrier((weighted, first))
            group_firsts.append(first)
            if r % GROUP == 0:
                opened = _halving_rest(jnp.stack(group_firsts, axis=1), "dp", 2)
                group_firsts = []
        if second is not None and r % GROUP == GROUP - 1:
            weighted, second = lax.optimization_barrier((weighted, second))
            moments.append(second)
            second = None
        if opened is not None:
            second = opened
        pieces = jnp.einsum("nk,njd->jkd", weighted, points3, preferred_element_type=jnp.float32)
        first = _halving_step(pieces, "dp", 1) if ndp > 1 else pieces
        log_total.append(row_top + jnp.log(row_total))
    group_firsts.append(first)
    if second is not None:
        moments.append(second)
    moments.append(_halving_rest(jnp.stack(group_firsts, axis=1), "dp", 2))
    moments = jnp.concatenate(moments, axis=0)
    mass = _all_reduce_doubling(jnp.stack(masses), "dp")
    own_slice = lax.dynamic_slice_in_dim(centroids, position * slab_width, slab_width, 2).astype(
        jnp.float32
    )
    updated = (
        (moments + prior_weight * own_slice) / (mass[:, :, None] + prior_weight)
    ).astype(jnp.bfloat16)
    summed = _all_reduce_doubling(sum(log_total), "rep")
    replicas = rep_local * lax.axis_size("rep")
    clusters = cent_local * lax.axis_size("cent")
    bagged_score = summed / replicas - math.log(clusters)
    return (updated, bagged_score)


def solution(mesh):
    return jax.shard_map(
        shards,
        mesh=mesh,
        in_specs=(P("dp", None), P("rep", "cent", None), P("rep", "dp")),
        out_specs=(P("rep", "cent", "dp"), P("dp")),
        check_vma=False,
    )
```

```python
import math

import jax
import jax.numpy as jnp
from jax import lax
from jax.sharding import PartitionSpec as P

prior_weight = 1.0


def _softmax_stats(top, total, axis):
    n = lax.axis_size(axis)
    index = lax.axis_index(axis)
    stats = jnp.stack([top, total])
    shifted = [stats]
    for s in range(1, n):
        shifted.append(lax.ppermute(stats, axis, [(i, (i + s) % n) for i in range(n)]))
    shifted = jnp.stack(shifted)
    ordered = jnp.take(shifted, (index - jnp.arange(n)) % n, axis=0)
    row_top = jnp.max(ordered[:, 0], axis=0)
    row_total = jnp.sum(ordered[:, 1] * jnp.exp(ordered[:, 0] - row_top[None]), axis=0)
    return row_top, row_total


def _all_reduce_doubling(x, axis):
    n = lax.axis_size(axis)
    if n & (n - 1):
        return lax.psum(x, axis)
    b = 1
    while b < n:
        x = x + lax.ppermute(x, axis, [(i, i ^ b) for i in range(n)])
        b *= 2
    return x


def _halving_step(pieces, axis, b):
    n = lax.axis_size(axis)
    m = pieces.shape[0] // 2
    view = pieces.reshape((m, 2) + pieces.shape[1:])
    mine = (lax.axis_index(axis) // b) % 2
    keep = lax.dynamic_index_in_dim(view, mine, axis=1, keepdims=False)
    send = lax.dynamic_index_in_dim(view, 1 - mine, axis=1, keepdims=False)
    return keep + lax.ppermute(send, axis, [(i, i ^ b) for i in range(n)])


def _halving_rest(pieces, axis, b):
    n = lax.axis_size(axis)
    while b < n:
        pieces = _halving_step(pieces, axis, b)
        b *= 2
    return pieces[0]


def shards(points, centroids, counts):
    rep_local, cent_local, features = centroids.shape
    ndp = lax.axis_size("dp")
    slab_width = features // ndp
    position = lax.axis_index("dp")
    points3 = points.reshape(points.shape[0], ndp, slab_width)
    squares = jnp.sum(jnp.square(centroids.astype(jnp.float32)), axis=2)
    all_logits = [
        jnp.dot(points, centroids[r].T, preferred_element_type=jnp.float32)
        - 0.5 * squares[r][None, :]
        for r in range(rep_local)
    ]
    local_top = jnp.stack([jnp.max(l, axis=1) for l in all_logits])
    local_total = jnp.stack(
        [jnp.sum(jnp.exp(l - t[:, None]), axis=1) for l, t in zip(all_logits, local_top)]
    )
    tops, totals = _softmax_stats(local_top, local_total, "cent")
    weights = counts.astype(jnp.float32)
    weighted = [
        (
            jnp.exp(all_logits[r] - tops[r][:, None]) / totals[r][:, None] * weights[r][:, None]
        ).astype(jnp.bfloat16)
        for r in range(rep_local)
    ]
    mass = _all_reduce_doubling(
        jnp.stack([jnp.sum(w.astype(jnp.float32), axis=0) for w in weighted]), "dp"
    )
    head = jnp.einsum("nk,njd->jkd", weighted[0], points3, preferred_element_type=jnp.float32)
    head = _halving_rest(head, "dp", 1)[None]
    moments = [head]
    if rep_local > 1:
        rest = jnp.einsum(
            "rnk,njd->jrkd", jnp.stack(weighted[1:]), points3, preferred_element_type=jnp.float32
        )
        rest, head = lax.optimization_barrier((rest, head))
        moments = [head, _halving_rest(rest, "dp", 1)]
    moments = jnp.concatenate(moments, axis=0)
    own_slice = lax.dynamic_slice_in_dim(centroids, position * slab_width, slab_width, 2).astype(
        jnp.float32
    )
    updated = (
        (moments + prior_weight * own_slice) / (mass[:, :, None] + prior_weight)
    ).astype(jnp.bfloat16)
    log_total = tops + jnp.log(totals)
    summed = _all_reduce_doubling(jnp.sum(log_total, axis=0), "rep")
    replicas = rep_local * lax.axis_size("rep")
    clusters = cent_local * lax.axis_size("cent")
    bagged_score = summed / replicas - math.log(clusters)
    return (updated, bagged_score)


def solution(mesh):
    return jax.shard_map(
        shards,
        mesh=mesh,
        in_specs=(P("dp", None), P("rep", "cent", None), P("rep", "dp")),
        out_specs=(P("rep", "cent", "dp"), P("dp")),
        check_vma=False,
    )
```

```python
import math

import jax
import jax.numpy as jnp
from jax import lax
from jax.sharding import PartitionSpec as P

prior_weight = 1.0


def _softmax_stats(top, total, axis):
    n = lax.axis_size(axis)
    index = lax.axis_index(axis)
    stats = jnp.stack([top, total])
    shifted = [stats]
    for s in range(1, n):
        shifted.append(lax.ppermute(stats, axis, [(i, (i + s) % n) for i in range(n)]))
    shifted = jnp.stack(shifted)
    ordered = jnp.take(shifted, (index - jnp.arange(n)) % n, axis=0)
    row_top = jnp.max(ordered[:, 0], axis=0)
    row_total = jnp.sum(ordered[:, 1] * jnp.exp(ordered[:, 0] - row_top[None]), axis=0)
    return row_top, row_total


def _all_reduce_doubling(x, axis):
    n = lax.axis_size(axis)
    if n & (n - 1):
        return lax.psum(x, axis)
    b = 1
    while b < n:
        x = x + lax.ppermute(x, axis, [(i, i ^ b) for i in range(n)])
        b *= 2
    return x


def _halving_step(pieces, axis, b):
    n = lax.axis_size(axis)
    m = pieces.shape[0] // 2
    view = pieces.reshape((m, 2) + pieces.shape[1:])
    mine = (lax.axis_index(axis) // b) % 2
    keep = lax.dynamic_index_in_dim(view, mine, axis=1, keepdims=False)
    send = lax.dynamic_index_in_dim(view, 1 - mine, axis=1, keepdims=False)
    return keep + lax.ppermute(send, axis, [(i, i ^ b) for i in range(n)])


def _halving_rest(pieces, axis, b):
    n = lax.axis_size(axis)
    while b < n:
        pieces = _halving_step(pieces, axis, b)
        b *= 2
    return pieces[0]


def shards(points, centroids, counts):
    rep_local, cent_local, features = centroids.shape
    ndp = lax.axis_size("dp")
    slab_width = features // ndp
    position = lax.axis_index("dp")
    points3 = points.reshape(points.shape[0], ndp, slab_width)
    squares = jnp.sum(jnp.square(centroids.astype(jnp.float32)), axis=2)
    all_logits = [
        jnp.dot(points, centroids[r].T, preferred_element_type=jnp.float32)
        - 0.5 * squares[r][None, :]
        for r in range(rep_local)
    ]
    local_top = jnp.stack([jnp.max(l, axis=1) for l in all_logits])
    local_total = jnp.stack(
        [jnp.sum(jnp.exp(l - t[:, None]), axis=1) for l, t in zip(all_logits, local_top)]
    )
    tops, totals = _softmax_stats(local_top, local_total, "cent")
    weights = counts.astype(jnp.float32)
    weighted = [
        (
            jnp.exp(all_logits[r] - tops[r][:, None]) / totals[r][:, None] * weights[r][:, None]
        ).astype(jnp.bfloat16)
        for r in range(rep_local)
    ]
    mass = _all_reduce_doubling(
        jnp.stack([jnp.sum(w.astype(jnp.float32), axis=0) for w in weighted]), "dp"
    )
    head = jnp.einsum("nk,njd->jkd", weighted[0], points3, preferred_element_type=jnp.float32)
    head = _halving_rest(head, "dp", 1)[None]
    moments = [head]
    if rep_local > 1:
        rest = jnp.einsum(
            "rnk,njd->jrkd", jnp.stack(weighted[1:]), points3, preferred_element_type=jnp.float32
        )
        rest = _halving_step(rest, "dp", 1) if ndp > 1 else rest
        rest, head = lax.optimization_barrier((rest, head))
        moments = [head, _halving_rest(rest, "dp", 2)]
    moments = jnp.concatenate(moments, axis=0)
    own_slice = lax.dynamic_slice_in_dim(centroids, position * slab_width, slab_width, 2).astype(
        jnp.float32
    )
    updated = (
        (moments + prior_weight * own_slice) / (mass[:, :, None] + prior_weight)
    ).astype(jnp.bfloat16)
    log_total = tops + jnp.log(totals)
    summed = _all_reduce_doubling(jnp.sum(log_total, axis=0), "rep")
    replicas = rep_local * lax.axis_size("rep")
    clusters = cent_local * lax.axis_size("cent")
    bagged_score = summed / replicas - math.log(clusters)
    return (updated, bagged_score)


def solution(mesh):
    return jax.shard_map(
        shards,
        mesh=mesh,
        in_specs=(P("dp", None), P("rep", "cent", None), P("rep", "dp")),
        out_specs=(P("rep", "cent", "dp"), P("dp")),
        check_vma=False,
    )
```

```python
import math

import jax
import jax.numpy as jnp
from jax import lax
from jax.sharding import PartitionSpec as P

prior_weight = 1.0


def _softmax_stats(top, total, axis):
    n = lax.axis_size(axis)
    index = lax.axis_index(axis)
    stats = jnp.stack([top, total])
    shifted = [stats]
    for s in range(1, n):
        shifted.append(lax.ppermute(stats, axis, [(i, (i + s) % n) for i in range(n)]))
    shifted = jnp.stack(shifted)
    ordered = jnp.take(shifted, (index - jnp.arange(n)) % n, axis=0)
    row_top = jnp.max(ordered[:, 0], axis=0)
    row_total = jnp.sum(ordered[:, 1] * jnp.exp(ordered[:, 0] - row_top[None]), axis=0)
    return row_top, row_total


def _all_reduce_doubling(x, axis):
    n = lax.axis_size(axis)
    if n & (n - 1):
        return lax.psum(x, axis)
    b = 1
    while b < n:
        x = x + lax.ppermute(x, axis, [(i, i ^ b) for i in range(n)])
        b *= 2
    return x


def _halving_step(pieces, axis, b):
    n = lax.axis_size(axis)
    m = pieces.shape[0] // 2
    view = pieces.reshape((m, 2) + pieces.shape[1:])
    mine = (lax.axis_index(axis) // b) % 2
    keep = lax.dynamic_index_in_dim(view, mine, axis=1, keepdims=False)
    send = lax.dynamic_index_in_dim(view, 1 - mine, axis=1, keepdims=False)
    return keep + lax.ppermute(send, axis, [(i, i ^ b) for i in range(n)])


def _halving_rest(pieces, axis, b):
    n = lax.axis_size(axis)
    while b < n:
        pieces = _halving_step(pieces, axis, b)
        b *= 2
    return pieces[0]


def shards(points, centroids, counts):
    rep_local, cent_local, features = centroids.shape
    ndp = lax.axis_size("dp")
    slab_width = features // ndp
    position = lax.axis_index("dp")
    points3 = points.reshape(points.shape[0], ndp, slab_width)
    squares = jnp.sum(jnp.square(centroids.astype(jnp.float32)), axis=2)
    all_logits = [
        jnp.dot(points, centroids[r].T, preferred_element_type=jnp.float32)
        - 0.5 * squares[r][None, :]
        for r in range(rep_local)
    ]
    local_top = jnp.stack([jnp.max(l, axis=1) for l in all_logits])
    local_total = jnp.stack(
        [jnp.sum(jnp.exp(l - t[:, None]), axis=1) for l, t in zip(all_logits, local_top)]
    )
    tops, totals = _softmax_stats(local_top, local_total, "cent")
    weights = counts.astype(jnp.float32)
    weighted = [
        (
            jnp.exp(all_logits[r] - tops[r][:, None]) / totals[r][:, None] * weights[r][:, None]
        ).astype(jnp.bfloat16)
        for r in range(rep_local)
    ]
    mass = _all_reduce_doubling(
        jnp.stack([jnp.sum(w.astype(jnp.float32), axis=0) for w in weighted]), "dp"
    )
    head = jnp.einsum("nk,njd->jkd", weighted[0], points3, preferred_element_type=jnp.float32)
    head = _halving_rest(head, "dp", 1)[None]
    moments = [head]
    if rep_local > 1:
        others = jnp.stack(weighted[1:])
        if ndp > 1:
            pairs = points3.reshape(points3.shape[0], ndp // 2, 2, slab_width)
            mine = position % 2
            sent = jnp.einsum(
                "rnk,naw->arkw",
                others,
                lax.dynamic_index_in_dim(pairs, 1 - mine, axis=2, keepdims=False),
                preferred_element_type=jnp.float32,
            )
            received = lax.ppermute(sent, "dp", [(i, i ^ 1) for i in range(ndp)])
            received, head = lax.optimization_barrier((received, head))
            kept = jnp.einsum(
                "rnk,naw->arkw",
                others,
                lax.dynamic_index_in_dim(pairs, mine, axis=2, keepdims=False),
                preferred_element_type=jnp.float32,
            )
            moments = [head, _halving_rest(kept + received, "dp", 2)]
        else:
            moments = [head, jnp.einsum("rnk,nd->rkd", others, points, preferred_element_type=jnp.float32)]
    moments = jnp.concatenate(moments, axis=0)
    own_slice = lax.dynamic_slice_in_dim(centroids, position * slab_width, slab_width, 2).astype(
        jnp.float32
    )
    updated = (
        (moments + prior_weight * own_slice) / (mass[:, :, None] + prior_weight)
    ).astype(jnp.bfloat16)
    log_total = tops + jnp.log(totals)
    summed = _all_reduce_doubling(jnp.sum(log_total, axis=0), "rep")
    replicas = rep_local * lax.axis_size("rep")
    clusters = cent_local * lax.axis_size("cent")
    bagged_score = summed / replicas - math.log(clusters)
    return (updated, bagged_score)


def solution(mesh):
    return jax.shard_map(
        shards,
        mesh=mesh,
        in_specs=(P("dp", None), P("rep", "cent", None), P("rep", "dp")),
        out_specs=(P("rep", "cent", "dp"), P("dp")),
        check_vma=False,
    )
```

```python
import math

import jax
import jax.numpy as jnp
from jax import lax
from jax.sharding import PartitionSpec as P

prior_weight = 1.0


def _softmax_stats(top, total, axis):
    n = lax.axis_size(axis)
    index = lax.axis_index(axis)
    stats = jnp.stack([top, total])
    shifted = [stats]
    for s in range(1, n):
        shifted.append(lax.ppermute(stats, axis, [(i, (i + s) % n) for i in range(n)]))
    shifted = jnp.stack(shifted)
    ordered = jnp.take(shifted, (index - jnp.arange(n)) % n, axis=0)
    row_top = jnp.max(ordered[:, 0], axis=0)
    row_total = jnp.sum(ordered[:, 1] * jnp.exp(ordered[:, 0] - row_top[None]), axis=0)
    return row_top, row_total


def _all_reduce_doubling(x, axis):
    n = lax.axis_size(axis)
    if n & (n - 1):
        return lax.psum(x, axis)
    b = 1
    while b < n:
        x = x + lax.ppermute(x, axis, [(i, i ^ b) for i in range(n)])
        b *= 2
    return x


def _halving_step(pieces, axis, b):
    n = lax.axis_size(axis)
    m = pieces.shape[0] // 2
    view = pieces.reshape((m, 2) + pieces.shape[1:])
    mine = (lax.axis_index(axis) // b) % 2
    keep = lax.dynamic_index_in_dim(view, mine, axis=1, keepdims=False)
    send = lax.dynamic_index_in_dim(view, 1 - mine, axis=1, keepdims=False)
    return keep + lax.ppermute(send, axis, [(i, i ^ b) for i in range(n)])


def _halving_rest(pieces, axis, b):
    n = lax.axis_size(axis)
    while b < n:
        pieces = _halving_step(pieces, axis, b)
        b *= 2
    return pieces[0]


def shards(points, centroids, counts):
    rep_local, cent_local, features = centroids.shape
    ndp = lax.axis_size("dp")
    slab_width = features // ndp
    position = lax.axis_index("dp")
    points3 = points.reshape(points.shape[0], ndp, slab_width)
    squares = jnp.sum(jnp.square(centroids.astype(jnp.float32)), axis=2)
    all_logits = [
        jnp.dot(points, centroids[r].T, preferred_element_type=jnp.float32)
        - 0.5 * squares[r][None, :]
        for r in range(rep_local)
    ]
    local_top = jnp.stack([jnp.max(l, axis=1) for l in all_logits])
    local_total = jnp.stack(
        [jnp.sum(jnp.exp(l - t[:, None]), axis=1) for l, t in zip(all_logits, local_top)]
    )
    tops, totals = _softmax_stats(local_top, local_total, "cent")
    weights = counts.astype(jnp.float32)
    weighted = [
        (
            jnp.exp(all_logits[r] - tops[r][:, None]) / totals[r][:, None] * weights[r][:, None]
        ).astype(jnp.bfloat16)
        for r in range(rep_local)
    ]
    mass = _all_reduce_doubling(
        jnp.stack([jnp.sum(w.astype(jnp.float32), axis=0) for w in weighted]), "dp"
    )
    head = jnp.einsum("nk,njd->jkd", weighted[0], points3, preferred_element_type=jnp.float32)
    head = _halving_rest(head, "dp", 1)[None]
    moments = [head]
    if rep_local > 1:
        rest = jnp.einsum(
            "rnk,njd->jrkd", jnp.stack(weighted[1:]), points3, preferred_element_type=jnp.float32
        )
        rest, head = lax.optimization_barrier((rest, head))
        moments = [head, _halving_rest(rest, "dp", 1)]
    own_slice = lax.dynamic_slice_in_dim(centroids, position * slab_width, slab_width, 2).astype(
        jnp.float32
    )
    updated = []
    start = 0
    for part in moments:
        stop = start + part.shape[0]
        updated.append(
            (
                (part + prior_weight * own_slice[start:stop])
                / (mass[start:stop, :, None] + prior_weight)
            ).astype(jnp.bfloat16)
        )
        start = stop
    updated = jnp.concatenate(updated, axis=0)
    log_total = tops + jnp.log(totals)
    summed = _all_reduce_doubling(jnp.sum(log_total, axis=0), "rep")
    replicas = rep_local * lax.axis_size("rep")
    clusters = cent_local * lax.axis_size("cent")
    bagged_score = summed / replicas - math.log(clusters)
    return (updated, bagged_score)


def solution(mesh):
    return jax.shard_map(
        shards,
        mesh=mesh,
        in_specs=(P("dp", None), P("rep", "cent", None), P("rep", "dp")),
        out_specs=(P("rep", "cent", "dp"), P("dp")),
        check_vma=False,
    )
```

```python
import math

import jax
import jax.numpy as jnp
from jax import lax
from jax.sharding import PartitionSpec as P

prior_weight = 1.0


def _softmax_stats(top, total, axis):
    n = lax.axis_size(axis)
    index = lax.axis_index(axis)
    stats = jnp.stack([top, total])
    shifted = [stats]
    for s in range(1, n):
        shifted.append(lax.ppermute(stats, axis, [(i, (i + s) % n) for i in range(n)]))
    shifted = jnp.stack(shifted)
    ordered = jnp.take(shifted, (index - jnp.arange(n)) % n, axis=0)
    row_top = jnp.max(ordered[:, 0], axis=0)
    row_total = jnp.sum(ordered[:, 1] * jnp.exp(ordered[:, 0] - row_top[None]), axis=0)
    return row_top, row_total


def _all_reduce_doubling(x, axis):
    n = lax.axis_size(axis)
    if n & (n - 1):
        return lax.psum(x, axis)
    b = 1
    while b < n:
        x = x + lax.ppermute(x, axis, [(i, i ^ b) for i in range(n)])
        b *= 2
    return x


def _halving_step(pieces, axis, b):
    n = lax.axis_size(axis)
    m = pieces.shape[0] // 2
    view = pieces.reshape((m, 2) + pieces.shape[1:])
    mine = (lax.axis_index(axis) // b) % 2
    keep = lax.dynamic_index_in_dim(view, mine, axis=1, keepdims=False)
    send = lax.dynamic_index_in_dim(view, 1 - mine, axis=1, keepdims=False)
    return keep + lax.ppermute(send, axis, [(i, i ^ b) for i in range(n)])


def _halving_rest(pieces, axis, b):
    n = lax.axis_size(axis)
    while b < n:
        pieces = _halving_step(pieces, axis, b)
        b *= 2
    return pieces[0]


def shards(points, centroids, counts):
    rep_local, cent_local, features = centroids.shape
    ndp = lax.axis_size("dp")
    slab_width = features // ndp
    position = lax.axis_index("dp")
    points3 = points.reshape(points.shape[0], ndp, slab_width)
    squares = jnp.sum(jnp.square(centroids.astype(jnp.float32)), axis=2)
    all_logits = [
        jnp.dot(points, centroids[r].T, preferred_element_type=jnp.float32)
        - 0.5 * squares[r][None, :]
        for r in range(rep_local)
    ]
    local_top = jnp.stack([jnp.max(l, axis=1) for l in all_logits])
    local_total = jnp.stack(
        [jnp.sum(jnp.exp(l - t[:, None]), axis=1) for l, t in zip(all_logits, local_top)]
    )
    tops, totals = _softmax_stats(local_top, local_total, "cent")
    weights = counts.astype(jnp.float32)
    weighted = [
        (
            jnp.exp(all_logits[r] - tops[r][:, None]) / totals[r][:, None] * weights[r][:, None]
        ).astype(jnp.bfloat16)
        for r in range(rep_local)
    ]
    mass_logits, mass_tops, mass_totals = lax.optimization_barrier((all_logits, tops, totals))
    mass = _all_reduce_doubling(
        jnp.stack(
            [
                jnp.sum(
                    (
                        jnp.exp(mass_logits[r] - mass_tops[r][:, None])
                        / mass_totals[r][:, None]
                        * weights[r][:, None]
                    )
                    .astype(jnp.bfloat16)
                    .astype(jnp.float32),
                    axis=0,
                )
                for r in range(rep_local)
            ]
        ),
        "dp",
    )
    head = jnp.einsum("nk,njd->jkd", weighted[0], points3, preferred_element_type=jnp.float32)
    head = _halving_rest(head, "dp", 1)[None]
    moments = [head]
    if rep_local > 1:
        rest = jnp.einsum(
            "rnk,njd->jrkd", jnp.stack(weighted[1:]), points3, preferred_element_type=jnp.float32
        )
        rest, head = lax.optimization_barrier((rest, head))
        moments = [head, _halving_rest(rest, "dp", 1)]
    moments = jnp.concatenate(moments, axis=0)
    own_slice = lax.dynamic_slice_in_dim(centroids, position * slab_width, slab_width, 2).astype(
        jnp.float32
    )
    updated = (
        (moments + prior_weight * own_slice) / (mass[:, :, None] + prior_weight)
    ).astype(jnp.bfloat16)
    log_total = tops + jnp.log(totals)
    summed = _all_reduce_doubling(jnp.sum(log_total, axis=0), "rep")
    replicas = rep_local * lax.axis_size("rep")
    clusters = cent_local * lax.axis_size("cent")
    bagged_score = summed / replicas - math.log(clusters)
    return (updated, bagged_score)


def solution(mesh):
    return jax.shard_map(
        shards,
        mesh=mesh,
        in_specs=(P("dp", None), P("rep", "cent", None), P("rep", "dp")),
        out_specs=(P("rep", "cent", "dp"), P("dp")),
        check_vma=False,
    )
```

```python
import math

import jax
import jax.numpy as jnp
from jax import lax
from jax.sharding import PartitionSpec as P

prior_weight = 1.0


def _softmax_stats(top, total, axis):
    n = lax.axis_size(axis)
    index = lax.axis_index(axis)
    stats = jnp.stack([top, total])
    shifted = [stats]
    for s in range(1, n):
        shifted.append(lax.ppermute(stats, axis, [(i, (i + s) % n) for i in range(n)]))
    shifted = jnp.stack(shifted)
    ordered = jnp.take(shifted, (index - jnp.arange(n)) % n, axis=0)
    row_top = jnp.max(ordered[:, 0], axis=0)
    row_total = jnp.sum(ordered[:, 1] * jnp.exp(ordered[:, 0] - row_top[None]), axis=0)
    return row_top, row_total


def _all_reduce_doubling(x, axis):
    n = lax.axis_size(axis)
    if n & (n - 1):
        return lax.psum(x, axis)
    b = 1
    while b < n:
        x = x + lax.ppermute(x, axis, [(i, i ^ b) for i in range(n)])
        b *= 2
    return x


def _halving_step(pieces, axis, b):
    n = lax.axis_size(axis)
    m = pieces.shape[0] // 2
    view = pieces.reshape((m, 2) + pieces.shape[1:])
    mine = (lax.axis_index(axis) // b) % 2
    keep = lax.dynamic_index_in_dim(view, mine, axis=1, keepdims=False)
    send = lax.dynamic_index_in_dim(view, 1 - mine, axis=1, keepdims=False)
    return keep + lax.ppermute(send, axis, [(i, i ^ b) for i in range(n)])


def _halving_rest(pieces, axis, b):
    n = lax.axis_size(axis)
    while b < n:
        pieces = _halving_step(pieces, axis, b)
        b *= 2
    return pieces[0]


def shards(points, centroids, counts):
    rep_local, cent_local, features = centroids.shape
    ndp = lax.axis_size("dp")
    slab_width = features // ndp
    position = lax.axis_index("dp")
    points3 = points.reshape(points.shape[0], ndp, slab_width)
    squares = jnp.sum(jnp.square(centroids.astype(jnp.float32)), axis=2)
    all_logits = [
        jnp.dot(points, centroids[r].T, preferred_element_type=jnp.float32)
        - 0.5 * squares[r][None, :]
        for r in range(rep_local)
    ]
    local_top = jnp.stack([jnp.max(l, axis=1) for l in all_logits])
    local_total = jnp.stack(
        [jnp.sum(jnp.exp(l - t[:, None]), axis=1) for l, t in zip(all_logits, local_top)]
    )
    tops, totals = _softmax_stats(local_top, local_total, "cent")
    weights = counts.astype(jnp.float32)
    weighted = [
        (
            jnp.exp(all_logits[r] - tops[r][:, None]) / totals[r][:, None] * weights[r][:, None]
        ).astype(jnp.bfloat16)
        for r in range(rep_local)
    ]
    head = jnp.einsum("nk,njd->jkd", weighted[0], points3, preferred_element_type=jnp.float32)
    head = _halving_rest(head, "dp", 1)[None]
    moments = [head]
    if rep_local > 1:
        rest = jnp.einsum(
            "rnk,njd->jrkd", jnp.stack(weighted[1:]), points3, preferred_element_type=jnp.float32
        )
        rest, head = lax.optimization_barrier((rest, head))
        moments = [head, _halving_rest(rest, "dp", 1)]
    moments = jnp.concatenate(moments, axis=0)
    mass_logits, mass_tops, mass_totals, _ = lax.optimization_barrier(
        (all_logits, tops, totals, moments[:1])
    )
    mass = _all_reduce_doubling(
        jnp.stack(
            [
                jnp.sum(
                    (
                        jnp.exp(mass_logits[r] - mass_tops[r][:, None])
                        / mass_totals[r][:, None]
                        * weights[r][:, None]
                    )
                    .astype(jnp.bfloat16)
                    .astype(jnp.float32),
                    axis=0,
                )
                for r in range(rep_local)
            ]
        ),
        "dp",
    )
    own_slice = lax.dynamic_slice_in_dim(centroids, position * slab_width, slab_width, 2).astype(
        jnp.float32
    )
    updated = (
        (moments + prior_weight * own_slice) / (mass[:, :, None] + prior_weight)
    ).astype(jnp.bfloat16)
    log_total = tops + jnp.log(totals)
    summed = _all_reduce_doubling(jnp.sum(log_total, axis=0), "rep")
    replicas = rep_local * lax.axis_size("rep")
    clusters = cent_local * lax.axis_size("cent")
    bagged_score = summed / replicas - math.log(clusters)
    return (updated, bagged_score)


def solution(mesh):
    return jax.shard_map(
        shards,
        mesh=mesh,
        in_specs=(P("dp", None), P("rep", "cent", None), P("rep", "dp")),
        out_specs=(P("rep", "cent", "dp"), P("dp")),
        check_vma=False,
    )
```

```python
import math

import jax
import jax.numpy as jnp
from jax import lax
from jax.sharding import PartitionSpec as P

prior_weight = 1.0


def _softmax_stats(top, total, axis):
    n = lax.axis_size(axis)
    index = lax.axis_index(axis)
    stats = jnp.stack([top, total])
    shifted = [stats]
    for s in range(1, n):
        shifted.append(lax.ppermute(stats, axis, [(i, (i + s) % n) for i in range(n)]))
    shifted = jnp.stack(shifted)
    ordered = jnp.take(shifted, (index - jnp.arange(n)) % n, axis=0)
    row_top = jnp.max(ordered[:, 0], axis=0)
    row_total = jnp.sum(ordered[:, 1] * jnp.exp(ordered[:, 0] - row_top[None]), axis=0)
    return row_top, row_total


def _all_reduce_doubling(x, axis):
    n = lax.axis_size(axis)
    if n & (n - 1):
        return lax.psum(x, axis)
    b = 1
    while b < n:
        x = x + lax.ppermute(x, axis, [(i, i ^ b) for i in range(n)])
        b *= 2
    return x


def _halving_step(pieces, axis, b):
    n = lax.axis_size(axis)
    m = pieces.shape[0] // 2
    view = pieces.reshape((m, 2) + pieces.shape[1:])
    mine = (lax.axis_index(axis) // b) % 2
    keep = lax.dynamic_index_in_dim(view, mine, axis=1, keepdims=False)
    send = lax.dynamic_index_in_dim(view, 1 - mine, axis=1, keepdims=False)
    return keep + lax.ppermute(send, axis, [(i, i ^ b) for i in range(n)])


def _halving_rest(pieces, axis, b):
    n = lax.axis_size(axis)
    while b < n:
        pieces = _halving_step(pieces, axis, b)
        b *= 2
    return pieces[0]


def shards(points, centroids, counts):
    rep_local, cent_local, features = centroids.shape
    ndp = lax.axis_size("dp")
    slab_width = features // ndp
    position = lax.axis_index("dp")
    points3 = points.reshape(points.shape[0], ndp, slab_width)
    squares = jnp.sum(jnp.square(centroids.astype(jnp.float32)), axis=2)
    def logits_of(center, square):
        return (
            jnp.dot(points, center.T, preferred_element_type=jnp.float32) - 0.5 * square[None, :]
        )

    later = [logits_of(centroids[r], squares[r]) for r in range(1, rep_local)]
    first_center, later = lax.optimization_barrier((centroids[0], later))
    all_logits = [logits_of(first_center, squares[0])] + list(later)
    local_top = jnp.stack([jnp.max(l, axis=1) for l in all_logits])
    local_total = jnp.stack(
        [jnp.sum(jnp.exp(l - t[:, None]), axis=1) for l, t in zip(all_logits, local_top)]
    )
    tops, totals = _softmax_stats(local_top, local_total, "cent")
    weights = counts.astype(jnp.float32)
    weighted = [
        (
            jnp.exp(all_logits[r] - tops[r][:, None]) / totals[r][:, None] * weights[r][:, None]
        ).astype(jnp.bfloat16)
        for r in range(rep_local)
    ]
    mass = _all_reduce_doubling(
        jnp.stack([jnp.sum(w.astype(jnp.float32), axis=0) for w in weighted]), "dp"
    )
    head = jnp.einsum("nk,njd->jkd", weighted[0], points3, preferred_element_type=jnp.float32)
    head = _halving_rest(head, "dp", 1)[None]
    moments = [head]
    if rep_local > 1:
        rest = jnp.einsum(
            "rnk,njd->jrkd", jnp.stack(weighted[1:]), points3, preferred_element_type=jnp.float32
        )
        rest, head = lax.optimization_barrier((rest, head))
        moments = [head, _halving_rest(rest, "dp", 1)]
    moments = jnp.concatenate(moments, axis=0)
    own_slice = lax.dynamic_slice_in_dim(centroids, position * slab_width, slab_width, 2).astype(
        jnp.float32
    )
    updated = (
        (moments + prior_weight * own_slice) / (mass[:, :, None] + prior_weight)
    ).astype(jnp.bfloat16)
    log_total = tops + jnp.log(totals)
    summed = _all_reduce_doubling(jnp.sum(log_total, axis=0), "rep")
    replicas = rep_local * lax.axis_size("rep")
    clusters = cent_local * lax.axis_size("cent")
    bagged_score = summed / replicas - math.log(clusters)
    return (updated, bagged_score)


def solution(mesh):
    return jax.shard_map(
        shards,
        mesh=mesh,
        in_specs=(P("dp", None), P("rep", "cent", None), P("rep", "dp")),
        out_specs=(P("rep", "cent", "dp"), P("dp")),
        check_vma=False,
    )
```

```python
import math

import jax
import jax.numpy as jnp
from jax import lax
from jax.sharding import PartitionSpec as P

prior_weight = 1.0


def _softmax_stats(top, total, axis):
    n = lax.axis_size(axis)
    index = lax.axis_index(axis)
    stats = jnp.stack([top, total])
    shifted = [stats]
    for s in range(1, n):
        shifted.append(lax.ppermute(stats, axis, [(i, (i + s) % n) for i in range(n)]))
    shifted = jnp.stack(shifted)
    ordered = jnp.take(shifted, (index - jnp.arange(n)) % n, axis=0)
    row_top = jnp.max(ordered[:, 0], axis=0)
    row_total = jnp.sum(ordered[:, 1] * jnp.exp(ordered[:, 0] - row_top[None]), axis=0)
    return row_top, row_total


def _all_reduce_doubling(x, axis):
    n = lax.axis_size(axis)
    if n & (n - 1):
        return lax.psum(x, axis)
    b = 1
    while b < n:
        x = x + lax.ppermute(x, axis, [(i, i ^ b) for i in range(n)])
        b *= 2
    return x


def _halving_step(pieces, axis, b):
    n = lax.axis_size(axis)
    m = pieces.shape[0] // 2
    view = pieces.reshape((m, 2) + pieces.shape[1:])
    mine = (lax.axis_index(axis) // b) % 2
    keep = lax.dynamic_index_in_dim(view, mine, axis=1, keepdims=False)
    send = lax.dynamic_index_in_dim(view, 1 - mine, axis=1, keepdims=False)
    return keep + lax.ppermute(send, axis, [(i, i ^ b) for i in range(n)])


def _halving_rest(pieces, axis, b):
    n = lax.axis_size(axis)
    if b >= n:
        return pieces[0]
    keep, received = None, None
    while b < n:
        m = pieces.shape[0] // 2 if keep is None else keep.shape[0] // 2
        mine = (lax.axis_index(axis) // b) % 2

        def half(x, t):
            view = x.reshape((m, 2) + x.shape[1:])
            return lax.dynamic_index_in_dim(view, t, axis=1, keepdims=False)

        if keep is None:
            send = half(pieces, 1 - mine)
            next_keep = half(pieces, mine)
        else:
            send = half(keep, 1 - mine) + half(received, 1 - mine)
            next_keep = half(keep, mine) + half(received, mine)
        received = lax.ppermute(send, axis, [(i, i ^ b) for i in range(n)])
        keep = next_keep
        b *= 2
    return (keep + received)[0]


def shards(points, centroids, counts):
    rep_local, cent_local, features = centroids.shape
    ndp = lax.axis_size("dp")
    slab_width = features // ndp
    position = lax.axis_index("dp")
    points3 = points.reshape(points.shape[0], ndp, slab_width)
    squares = jnp.sum(jnp.square(centroids.astype(jnp.float32)), axis=2)
    all_logits = [
        jnp.dot(points, centroids[r].T, preferred_element_type=jnp.float32)
        - 0.5 * squares[r][None, :]
        for r in range(rep_local)
    ]
    local_top = jnp.stack([jnp.max(l, axis=1) for l in all_logits])
    local_total = jnp.stack(
        [jnp.sum(jnp.exp(l - t[:, None]), axis=1) for l, t in zip(all_logits, local_top)]
    )
    tops, totals = _softmax_stats(local_top, local_total, "cent")
    weights = counts.astype(jnp.float32)
    weighted = [
        (
            jnp.exp(all_logits[r] - tops[r][:, None]) / totals[r][:, None] * weights[r][:, None]
        ).astype(jnp.bfloat16)
        for r in range(rep_local)
    ]
    mass = _all_reduce_doubling(
        jnp.stack([jnp.sum(w.astype(jnp.float32), axis=0) for w in weighted]), "dp"
    )
    head = jnp.einsum("nk,njd->jkd", weighted[0], points3, preferred_element_type=jnp.float32)
    head = _halving_rest(head, "dp", 1)[None]
    moments = [head]
    if rep_local > 1:
        rest = jnp.einsum(
            "rnk,njd->jrkd", jnp.stack(weighted[1:]), points3, preferred_element_type=jnp.float32
        )
        rest, head = lax.optimization_barrier((rest, head))
        moments = [head, _halving_rest(rest, "dp", 1)]
    moments = jnp.concatenate(moments, axis=0)
    own_slice = lax.dynamic_slice_in_dim(centroids, position * slab_width, slab_width, 2).astype(
        jnp.float32
    )
    updated = (
        (moments + prior_weight * own_slice) / (mass[:, :, None] + prior_weight)
    ).astype(jnp.bfloat16)
    log_total = tops + jnp.log(totals)
    summed = _all_reduce_doubling(jnp.sum(log_total, axis=0), "rep")
    replicas = rep_local * lax.axis_size("rep")
    clusters = cent_local * lax.axis_size("cent")
    bagged_score = summed / replicas - math.log(clusters)
    return (updated, bagged_score)


def solution(mesh):
    return jax.shard_map(
        shards,
        mesh=mesh,
        in_specs=(P("dp", None), P("rep", "cent", None), P("rep", "dp")),
        out_specs=(P("rep", "cent", "dp"), P("dp")),
        check_vma=False,
    )
```

```python
import math

import jax
import jax.numpy as jnp
from jax import lax
from jax.sharding import PartitionSpec as P

prior_weight = 1.0


def _softmax_stats(top, total, axis):
    n = lax.axis_size(axis)
    index = lax.axis_index(axis)
    stats = jnp.stack([top, total])
    shifted = [stats]
    for s in range(1, n):
        shifted.append(lax.ppermute(stats, axis, [(i, (i + s) % n) for i in range(n)]))
    shifted = jnp.stack(shifted)
    ordered = jnp.take(shifted, (index - jnp.arange(n)) % n, axis=0)
    row_top = jnp.max(ordered[:, 0], axis=0)
    row_total = jnp.sum(ordered[:, 1] * jnp.exp(ordered[:, 0] - row_top[None]), axis=0)
    return row_top, row_total


def _all_reduce_doubling(x, axis):
    n = lax.axis_size(axis)
    if n & (n - 1):
        return lax.psum(x, axis)
    b = 1
    while b < n:
        x = x + lax.ppermute(x, axis, [(i, i ^ b) for i in range(n)])
        b *= 2
    return x


def _halving_step(pieces, axis, b):
    n = lax.axis_size(axis)
    m = pieces.shape[0] // 2
    view = pieces.reshape((m, 2) + pieces.shape[1:])
    mine = (lax.axis_index(axis) // b) % 2
    keep = lax.dynamic_index_in_dim(view, mine, axis=1, keepdims=False)
    send = lax.dynamic_index_in_dim(view, 1 - mine, axis=1, keepdims=False)
    return keep + lax.ppermute(send, axis, [(i, i ^ b) for i in range(n)])


def _halving_rest(pieces, axis, b):
    n = lax.axis_size(axis)
    if b >= n:
        return pieces[0]
    keep, received = None, None
    while b < n:
        m = pieces.shape[0] // 2 if keep is None else keep.shape[0] // 2
        mine = (lax.axis_index(axis) // b) % 2

        def half(x, t):
            view = x.reshape((m, 2) + x.shape[1:])
            return lax.dynamic_index_in_dim(view, t, axis=1, keepdims=False)

        if keep is None:
            send = half(pieces, 1 - mine)
            next_keep = half(pieces, mine)
        else:
            send = half(keep, 1 - mine) + half(received, 1 - mine)
            next_keep = half(keep, mine) + half(received, mine)
        received = lax.ppermute(send, axis, [(i, i ^ b) for i in range(n)])
        keep = next_keep
        b *= 2
    return (keep + received)[0]


def shards(points, centroids, counts):
    rep_local, cent_local, features = centroids.shape
    ndp = lax.axis_size("dp")
    slab_width = features // ndp
    position = lax.axis_index("dp")
    points3 = points.reshape(points.shape[0], ndp, slab_width)
    squares = jnp.sum(jnp.square(centroids.astype(jnp.float32)), axis=2)
    all_logits = [
        jnp.dot(points, centroids[r].T, preferred_element_type=jnp.float32)
        - 0.5 * squares[r][None, :]
        for r in range(rep_local)
    ]
    local_top = jnp.stack([jnp.max(l, axis=1) for l in all_logits])
    local_total = jnp.stack(
        [jnp.sum(jnp.exp(l - t[:, None]), axis=1) for l, t in zip(all_logits, local_top)]
    )
    tops, totals = _softmax_stats(local_top, local_total, "cent")
    weights = counts.astype(jnp.float32)
    weighted = [
        (
            jnp.exp(all_logits[r] - tops[r][:, None]) / totals[r][:, None] * weights[r][:, None]
        ).astype(jnp.bfloat16)
        for r in range(rep_local)
    ]
    mass = _all_reduce_doubling(
        jnp.stack([jnp.sum(w.astype(jnp.float32), axis=0) for w in weighted]), "dp"
    )
    head = jnp.einsum("nk,njd->jkd", weighted[0], points3, preferred_element_type=jnp.float32)
    head = _halving_rest(head, "dp", 1)[None]
    moments = [head]
    if rep_local > 1:
        rest = jnp.einsum(
            "rnk,njd->jrkd", jnp.stack(weighted[1:]), points3, preferred_element_type=jnp.float32
        )
        rest, head = lax.optimization_barrier((rest, head))
        moments = [head, _halving_rest(rest, "dp", 1)]
    own_slice = lax.dynamic_slice_in_dim(centroids, position * slab_width, slab_width, 2).astype(
        jnp.float32
    )
    updated = []
    start = 0
    for part in moments:
        stop = start + part.shape[0]
        updated.append(
            (
                (part + prior_weight * own_slice[start:stop])
                / (mass[start:stop, :, None] + prior_weight)
            ).astype(jnp.bfloat16)
        )
        start = stop
    updated = jnp.concatenate(updated, axis=0)
    log_total = tops + jnp.log(totals)
    summed = _all_reduce_doubling(jnp.sum(log_total, axis=0), "rep")
    replicas = rep_local * lax.axis_size("rep")
    clusters = cent_local * lax.axis_size("cent")
    bagged_score = summed / replicas - math.log(clusters)
    return (updated, bagged_score)


def solution(mesh):
    return jax.shard_map(
        shards,
        mesh=mesh,
        in_specs=(P("dp", None), P("rep", "cent", None), P("rep", "dp")),
        out_specs=(P("rep", "cent", "dp"), P("dp")),
        check_vma=False,
    )
```

```python
import math

import jax
import jax.numpy as jnp
from jax import lax
from jax.sharding import PartitionSpec as P

prior_weight = 1.0


def _softmax_stats(top, total, axis):
    n = lax.axis_size(axis)
    index = lax.axis_index(axis)
    stats = jnp.stack([top, total])
    shifted = [stats]
    for s in range(1, n):
        shifted.append(lax.ppermute(stats, axis, [(i, (i + s) % n) for i in range(n)]))
    shifted = jnp.stack(shifted)
    ordered = jnp.take(shifted, (index - jnp.arange(n)) % n, axis=0)
    row_top = jnp.max(ordered[:, 0], axis=0)
    row_total = jnp.sum(ordered[:, 1] * jnp.exp(ordered[:, 0] - row_top[None]), axis=0)
    return row_top, row_total


def _all_reduce_doubling(x, axis):
    n = lax.axis_size(axis)
    if n & (n - 1):
        return lax.psum(x, axis)
    b = 1
    while b < n:
        x = x + lax.ppermute(x, axis, [(i, i ^ b) for i in range(n)])
        b *= 2
    return x


def _halving_step(pieces, axis, b):
    n = lax.axis_size(axis)
    m = pieces.shape[0] // 2
    view = pieces.reshape((m, 2) + pieces.shape[1:])
    mine = (lax.axis_index(axis) // b) % 2
    keep = lax.dynamic_index_in_dim(view, mine, axis=1, keepdims=False)
    send = lax.dynamic_index_in_dim(view, 1 - mine, axis=1, keepdims=False)
    return keep + lax.ppermute(send, axis, [(i, i ^ b) for i in range(n)])


def _halving_rest(pieces, axis, b):
    n = lax.axis_size(axis)
    if b >= n:
        return pieces[0]
    keep, received = None, None
    while b < n:
        m = pieces.shape[0] // 2 if keep is None else keep.shape[0] // 2
        mine = (lax.axis_index(axis) // b) % 2

        def half(x, t):
            view = x.reshape((m, 2) + x.shape[1:])
            return lax.dynamic_index_in_dim(view, t, axis=1, keepdims=False)

        if keep is None:
            send = half(pieces, 1 - mine)
            next_keep = half(pieces, mine)
        else:
            send = half(keep, 1 - mine) + half(received, 1 - mine)
            next_keep = half(keep, mine) + half(received, mine)
        received = lax.ppermute(send, axis, [(i, i ^ b) for i in range(n)])
        keep = next_keep
        b *= 2
    return (keep + received)[0]


def shards(points, centroids, counts):
    rep_local, cent_local, features = centroids.shape
    ndp = lax.axis_size("dp")
    slab_width = features // ndp
    position = lax.axis_index("dp")
    points3 = points.reshape(points.shape[0], ndp, slab_width)
    squares = jnp.sum(jnp.square(centroids.astype(jnp.float32)), axis=2)
    all_logits = [
        jnp.dot(points, centroids[r].T, preferred_element_type=jnp.float32)
        - 0.5 * squares[r][None, :]
        for r in range(rep_local)
    ]
    local_top = jnp.stack([jnp.max(l, axis=1) for l in all_logits])
    local_total = jnp.stack(
        [jnp.sum(jnp.exp(l - t[:, None]), axis=1) for l, t in zip(all_logits, local_top)]
    )
    tops, totals = _softmax_stats(local_top, local_total, "cent")
    weights = counts.astype(jnp.float32)
    weighted = [
        (
            jnp.exp(all_logits[r] - tops[r][:, None]) / totals[r][:, None] * weights[r][:, None]
        ).astype(jnp.bfloat16)
        for r in range(rep_local)
    ]
    mass_logits, mass_tops, mass_totals = lax.optimization_barrier((all_logits, tops, totals))
    mass = _all_reduce_doubling(
        jnp.stack(
            [
                jnp.sum(
                    (
                        jnp.exp(mass_logits[r] - mass_tops[r][:, None])
                        / mass_totals[r][:, None]
                        * weights[r][:, None]
                    )
                    .astype(jnp.bfloat16)
                    .astype(jnp.float32),
                    axis=0,
                )
                for r in range(rep_local)
            ]
        ),
        "dp",
    )
    head = jnp.einsum("nk,njd->jkd", weighted[0], points3, preferred_element_type=jnp.float32)
    head = _halving_rest(head, "dp", 1)[None]
    moments = [head]
    if rep_local > 1:
        rest = jnp.einsum(
            "rnk,njd->jrkd", jnp.stack(weighted[1:]), points3, preferred_element_type=jnp.float32
        )
        rest, head = lax.optimization_barrier((rest, head))
        moments = [head, _halving_rest(rest, "dp", 1)]
    moments = jnp.concatenate(moments, axis=0)
    own_slice = lax.dynamic_slice_in_dim(centroids, position * slab_width, slab_width, 2).astype(
        jnp.float32
    )
    updated = (
        (moments + prior_weight * own_slice) / (mass[:, :, None] + prior_weight)
    ).astype(jnp.bfloat16)
    log_total = tops + jnp.log(totals)
    summed = _all_reduce_doubling(jnp.sum(log_total, axis=0), "rep")
    replicas = rep_local * lax.axis_size("rep")
    clusters = cent_local * lax.axis_size("cent")
    bagged_score = summed / replicas - math.log(clusters)
    return (updated, bagged_score)


def solution(mesh):
    return jax.shard_map(
        shards,
        mesh=mesh,
        in_specs=(P("dp", None), P("rep", "cent", None), P("rep", "dp")),
        out_specs=(P("rep", "cent", "dp"), P("dp")),
        check_vma=False,
    )
```
